512 devices in a mesh: dp: 16 (over z), expert: 32 (over x, y, core).
Axes of the slice: x: 4, y: 4, z: 16, core: 2. Of those that a mesh axis runs over, the one named last changes fastest.
Arguments:
- x_tokens: bfloat16 [65536, 2048], P(('dp', 'expert')), may hold values from -6 to 6
- grad_out: bfloat16 [65536, 2048], P(('dp', 'expert')), may hold values from -6 to 6
- expert_ids: int32 [65536, 2], P(('dp', 'expert')), may hold values from 0 to 31, all different within a row; in each aligned block of 128 rows (0 to 127, 128 to 255, ...) at most 10 rows name the same one
- route_probs: float32 [65536, 2], P(('dp', 'expert')), may hold values from 0.1 to 1
- w_gate: bfloat16 [32, 2048, 768], P('expert', 'dp'), may hold values from -0.125 to 0.125
- w_up: bfloat16 [32, 2048, 768], P('expert', 'dp'), may hold values from -0.125 to 0.125
- w_down: bfloat16 [32, 2048, 768], P('expert', 'dp'), may hold values from -0.21875 to 0.21875
Outputs:
- grad_x: bfloat16 [65536, 2048], P(('dp', 'expert'))
- grad_probs: bfloat16 [65536, 2], P(('dp', 'expert'))
- grad_w_down: bfloat16 [32, 2048, 768], P('expert', 'dp')
The draws below stay inside these ranges and needn't reach their ends.
Inputs may be any that keep to these rules, and one draw needn't show every extreme that they name: `expert_ids`: each token names 2 different experts; among the 128 tokens of one device no expert is named by more than 10 routes, and in every draw some device names some expert exactly 10 times.
All inputs are finite; a program needn't handle non-finite values.
Results may differ from the reference program's by a relative error of at most 0.017.
Values may be sent and summed in bfloat16 or wider, within the bound.
No kernel may reach another device: no remote copies, remote signals or barrier semaphores. Data moves between devices by JAX's collectives and lax.ppermute only.
A program may use at most 64 MiB of HBM per device.

```python
import math
import jax
import jax.numpy as jnp
import numpy as np
from jax import lax

D = 2048
FF = 768
TOPK = 2
TOK_DEV = 128
EXPERTS = 32
CAP = 10
TOKENS = 65536
N_DP = 16
N_EXPERT = 32
DEVICES = 512


def shard_levels(key, shape, pieces, low, largest):
    gain = 1.0
    for position, parts in pieces:
        heights = jax.random.uniform(jax.random.fold_in(jax.random.fold_in(key, 6), position), (parts,), jnp.float32, low / len(pieces), largest / len(pieces))
        gain = gain * jnp.repeat(jnp.exp(heights), shape[position] // parts).reshape((-1,) + (1,) * (len(shape) - 1 - position))
    return gain


def deal_out(rng, own, number, rows, count, top, reach, skew):
    sequence = jax.random.permutation(rng, count)
    packed, ordinary = load_shares(count, rows * top, reach, skew, True), load_shares(count, rows * top, reach, skew, False)
    places = jnp.arange(count)

    def named(tallies, rotation):
        used = int((tallies > 0).sum())
        fixed = max(1, used // 4)
        moved = fixed + (places - fixed + rotation * (used - fixed)) % max(1, count - fixed)
        return jnp.zeros((count,), jnp.int32).at[sequence[jnp.where(places < fixed, places, moved)]].set(jnp.asarray(tallies, jnp.int32))

    tallies = jnp.where(number % 4 == 0, named(packed, number // 4), named(ordinary, number - number // 4 - 1))
    mixed = jax.random.permutation(jax.random.fold_in(own, 3), count)
    source_of, receiver = mixed[0:count // 2 * 2:2], mixed[1:count // 2 * 2:2]
    slack = jnp.minimum(tallies[source_of] - 1, reach - tallies[receiver]) // 2
    slack = jnp.where((source_of == sequence[0]) | (receiver == sequence[0]) | (tallies[receiver] == 0), 0, jnp.maximum(slack, 0))
    moved = jax.random.randint(jax.random.fold_in(own, 4), (count // 2,), 0, 1 << 20) % (slack + 1)
    tallies = tallies.at[source_of].add(-moved).at[receiver].add(moved)
    items = jnp.searchsorted(jnp.cumsum(tallies), jnp.arange(rows * top), side="right").astype(jnp.int32)
    listing = items.reshape(top, rows).T
    listing = listing[jax.random.permutation(jax.random.fold_in(own, 1), rows)]
    rotation = jax.random.randint(jax.random.fold_in(own, 2), (rows, 1), 0, top)
    return jnp.take_along_axis(listing, (jnp.arange(top)[None, :] + rotation) % top, axis=1)


def load_shares(count, total, most, skew, full):
    weights = [(1 << 20) // math.isqrt(standing ** skew) + 1 for standing in range(1, count + 1)]
    largest = most if full else min(most, max(-(-total // count), total * weights[0] // sum(weights)))
    least = 1 if total - largest >= count - 1 else 0
    holding, spare = [largest] + [least] * (count - 1), total - largest - least * (count - 1)
    while spare > 0:
        movable = [i for i in range(1, count) if holding[i] < largest] or [i for i in range(1, count) if holding[i] < most]
        whole, left = sum([weights[i] for i in movable]), spare
        for i in movable:
            addition = min(most - holding[i], max(1, left * weights[i] // whole), spare)
            holding[i] = holding[i] + addition
            spare = spare - addition
    return np.array(holding)


def normal_values(key, shape, width, reach, cuts=(), kind=jnp.bfloat16):
    array = width * jax.random.normal(key, shape, jnp.float32)
    if cuts:
        array = array * shard_levels(key, shape, cuts, -0.22, 0.18)
    return jnp.clip(array, -reach, reach).astype(kind)


def setup_inputs(seed: int = 0) -> dict:
    streams_of = jax.random.split(jax.random.key(seed), 8)
    x_tokens = normal_values(streams_of[0], (TOKENS, D), 1.0, 6.0, ((0, 512),))
    grad_out = normal_values(streams_of[1], (TOKENS, D), 1.0, 6.0, ((0, 512),))
    expert_ids_keys = jax.random.split(jax.random.fold_in(streams_of[2], 1), TOKENS // TOK_DEV)
    expert_ids_turns = jax.random.permutation(jax.random.fold_in(streams_of[2], 3), TOKENS // TOK_DEV)
    expert_ids = jax.vmap(lambda own, number: deal_out(jax.random.fold_in(streams_of[2], 2), own, number, TOK_DEV, EXPERTS, TOPK, CAP, 2))(expert_ids_keys, expert_ids_turns).reshape((TOKENS, TOPK))
    route_probs = jnp.clip(0.1 + 0.9 * jax.random.uniform(streams_of[3], (TOKENS, TOPK), jnp.float32) ** shard_levels(streams_of[3], (TOKENS, TOPK), ((0, 512),), -0.2, 0.2), 0.1, 1.0)
    w_gate = normal_values(streams_of[4], (EXPERTS, D, FF), D ** -0.5, 0.125, ((0, 32), (1, 16)))
    w_up = normal_values(streams_of[5], (EXPERTS, D, FF), D ** -0.5, 0.125, ((0, 32), (1, 16)))
    w_down = normal_values(streams_of[6], (EXPERTS, D, FF), FF ** -0.5, 0.21875, ((0, 32), (1, 16)))
    return {"x_tokens": x_tokens, "grad_out": grad_out, "expert_ids": expert_ids, "route_probs": route_probs, "w_gate": w_gate, "w_up": w_up, "w_down": w_down}


def reference(x_tokens, grad_out, expert_ids, route_probs, w_gate, w_up, w_down):
    routes = TOKENS * TOPK
    per_device = TOK_DEV * TOPK
    flat_ids = expert_ids.reshape(DEVICES, per_device)
    onehot = (flat_ids[:, :, None] == jnp.arange(EXPERTS, dtype=jnp.int32)).astype(jnp.int32)
    route_rank = jnp.sum((jnp.cumsum(onehot, axis=1) - onehot) * onehot, axis=2)
    device = jnp.arange(DEVICES, dtype=jnp.int32)[:, None]
    target = flat_ids * (DEVICES * CAP) + device * CAP + route_rank
    table = jnp.full((EXPERTS * DEVICES * CAP,), routes, jnp.int32)
    table = table.at[target.reshape(-1)].set(jnp.arange(routes, dtype=jnp.int32))
    table = table.reshape(EXPERTS, DEVICES * CAP)
    x_padded = jnp.concatenate([x_tokens, jnp.zeros((1, D), jnp.bfloat16)], axis=0)
    dy_padded = jnp.concatenate([grad_out, jnp.zeros((1, D), jnp.bfloat16)], axis=0)
    p_padded = jnp.concatenate([route_probs.reshape(-1), jnp.zeros((1,), jnp.float32)]).astype(jnp.bfloat16)

    def per_expert(totals, inputs):
        summed, prob_all = totals
        source, gate_w, up_w, down_w = inputs
        token_of = jnp.where(source < routes, source // TOPK, TOKENS).astype(jnp.int32)
        in_rows = x_padded[token_of]
        dy_rows = dy_padded[token_of]
        p_rows = p_padded[source].astype(jnp.float32)
        gate_pre = jnp.dot(in_rows, gate_w, preferred_element_type=jnp.float32)
        up_pre = jnp.dot(in_rows, up_w, preferred_element_type=jnp.float32)
        gate_sig = jax.nn.sigmoid(gate_pre)
        gate_act = gate_pre * gate_sig
        hidden = (gate_act * up_pre).astype(jnp.bfloat16)
        scaled = (p_rows[:, None] * dy_rows.astype(jnp.float32)).astype(jnp.bfloat16)
        out_rows = jnp.dot(hidden, down_w.T, preferred_element_type=jnp.float32)
        prob_slot = jnp.sum(dy_rows.astype(jnp.float32) * out_rows, axis=1).astype(jnp.bfloat16)
        hidden_grad = jnp.dot(scaled, down_w, preferred_element_type=jnp.float32)
        up_grad = (hidden_grad * gate_act).astype(jnp.bfloat16)
        gate_grad = (hidden_grad * up_pre * gate_sig * (1.0 + gate_pre * (1.0 - gate_sig))).astype(jnp.bfloat16)
        x_grad = (jnp.dot(gate_grad, gate_w.T, preferred_element_type=jnp.float32)
                  + jnp.dot(up_grad, up_w.T, preferred_element_type=jnp.float32)).astype(jnp.bfloat16)
        summed = summed.at[token_of].add(x_grad.astype(jnp.float32))
        prob_all = prob_all.at[source].set(prob_slot)
        grouped_s = scaled.reshape(N_DP, N_EXPERT * CAP, D).astype(jnp.float32)
        grouped_h = hidden.reshape(N_DP, N_EXPERT * CAP, FF).astype(jnp.float32)
        partial_sums = jnp.einsum('gsd,gsf->gdf', grouped_s, grouped_h).astype(jnp.bfloat16)
        partial_sums = lax.optimization_barrier(partial_sums)
        down_grad = jnp.sum(partial_sums.astype(jnp.float32), axis=0).astype(jnp.bfloat16)
        return (summed, prob_all), down_grad

    start_sum = jnp.zeros((TOKENS + 1, D), jnp.float32)
    start_prob = jnp.zeros((routes + 1,), jnp.bfloat16)
    (summed, prob_all), grad_w_down = lax.scan(per_expert, (start_sum, start_prob), (table, w_gate, w_up, w_down))
    grad_x = summed[:TOKENS].astype(jnp.bfloat16)
    grad_probs = prob_all[:routes].reshape(TOKENS, TOPK)
    return grad_x, grad_probs, grad_w_down
```

```python
import jax
import jax.numpy as jnp
from jax import lax
from jax.sharding import PartitionSpec as P


def ring_gather(shard, axis):
    n = lax.axis_size(axis)
    i = lax.axis_index(axis)
    rows = shard.shape[1]
    fwd = [(m, (m + 1) % n) for m in range(n)]
    bwd = [(m, (m - 1) % n) for m in range(n)]
    full = jnp.zeros((shard.shape[0], n * rows) + shard.shape[2:], shard.dtype)
    full = lax.dynamic_update_slice_in_dim(full, shard, i * rows, axis=1)
    f = shard
    b = shard
    for s in range(1, n // 2 + 1):
        f = lax.ppermute(f, axis, fwd)
        full = lax.dynamic_update_slice_in_dim(full, f, ((i - s) % n) * rows, axis=1)
        if s <= (n - 1) // 2:
            b = lax.ppermute(b, axis, bwd)
            full = lax.dynamic_update_slice_in_dim(full, b, ((i + s) % n) * rows, axis=1)
    return full


def ring_reduce_scatter(partial, axis):
    n = lax.axis_size(axis)
    i = lax.axis_index(axis)
    rows = partial.shape[0] // n
    fwd = [(m, (m + 1) % n) for m in range(n)]
    bwd = [(m, (m - 1) % n) for m in range(n)]

    def chunk(k):
        return lax.dynamic_slice_in_dim(partial, (k % n) * rows, rows, axis=0).astype(jnp.float32)

    total = chunk(i)
    nf = n // 2
    nb = (n - 1) // 2
    if nf > 0:
        acc = chunk(i + nf).astype(partial.dtype)
        for s in range(1, nf + 1):
            got = lax.ppermute(acc, axis, fwd)
            if s < nf:
                acc = (got.astype(jnp.float32) + chunk(i + nf - s)).astype(partial.dtype)
            else:
                total = total + got.astype(jnp.float32)
    if nb > 0:
        acc = chunk(i - nb).astype(partial.dtype)
        for s in range(1, nb + 1):
            got = lax.ppermute(acc, axis, bwd)
            if s < nb:
                acc = (got.astype(jnp.float32) + chunk(i - nb + s)).astype(partial.dtype)
            else:
                total = total + got.astype(jnp.float32)
    return total.astype(partial.dtype)


def per_device(x_tokens, grad_out, expert_ids, route_probs, w_gate, w_up, w_down):
    tok_count, model_width = x_tokens.shape
    top_count = expert_ids.shape[1]
    n_expert = lax.axis_size("expert")
    capacity = tok_count * top_count * 5 // (4 * n_expert)
    slot_count = n_expert * capacity
    routes = tok_count * top_count
    flat_ids = expert_ids.reshape(routes)
    onehot = (flat_ids[:, None] == jnp.arange(n_expert, dtype=jnp.int32)).astype(jnp.int32)
    route_rank = jnp.sum((jnp.cumsum(onehot, axis=0) - onehot) * onehot, axis=1)
    target = flat_ids * capacity + route_rank
    source = (
        jnp.full((slot_count,), routes, jnp.int32)
        .at[target]
        .set(jnp.arange(routes, dtype=jnp.int32))
    )
    token_of = jnp.where(source < routes, source // top_count, tok_count)
    x_padded = jnp.concatenate([x_tokens, jnp.zeros((1, model_width), jnp.bfloat16)], axis=0)
    dy_padded = jnp.concatenate([grad_out, jnp.zeros((1, model_width), jnp.bfloat16)], axis=0)
    p_padded = jnp.concatenate([route_probs.reshape(routes), jnp.zeros((1,), jnp.float32)]).astype(
        jnp.bfloat16
    )
    x_slots = x_padded[token_of].reshape(n_expert, capacity, model_width)
    dy_slots = dy_padded[token_of].reshape(n_expert, capacity, model_width)
    p_slots = p_padded[source].reshape(n_expert, capacity)
    arrived = (
        lax.all_to_all(x_slots, "expert", split_axis=0, concat_axis=0, tiled=True),
        lax.all_to_all(dy_slots, "expert", split_axis=0, concat_axis=0, tiled=True),
        lax.all_to_all(p_slots, "expert", split_axis=0, concat_axis=0, tiled=True),
    )
    in_rows = arrived[0].reshape(slot_count, model_width)
    dy_rows = arrived[1].reshape(slot_count, model_width)
    p_rows = arrived[2].reshape(slot_count).astype(jnp.float32)
    scaled = (p_rows[:, None] * dy_rows.astype(jnp.float32)).astype(jnp.bfloat16)
    full = ring_gather(jnp.stack([w_gate[0], w_up[0], w_down[0]]), "dp")
    gate_full = full[0]
    up_full = full[1]
    gate_pre = jnp.dot(in_rows, gate_full, preferred_element_type=jnp.float32)
    up_pre = jnp.dot(in_rows, up_full, preferred_element_type=jnp.float32)
    gate_sig = jax.nn.sigmoid(gate_pre)
    gate_act = gate_pre * gate_sig
    hidden = (gate_act * up_pre).astype(jnp.bfloat16)
    piece_rows = full[2]
    out_piece = jnp.dot(hidden, piece_rows.T, preferred_element_type=jnp.float32)
    grad_sum = jnp.dot(scaled, piece_rows, preferred_element_type=jnp.float32)
    prob_sum = jnp.sum(dy_rows.astype(jnp.float32) * out_piece, axis=1)
    hidden_grad, prob_sum = (grad_sum, prob_sum)
    up_grad = (hidden_grad * gate_act).astype(jnp.bfloat16)
    gate_grad = (hidden_grad * up_pre * gate_sig * (1.0 + gate_pre * (1.0 - gate_sig))).astype(
        jnp.bfloat16
    )
    x_grad = (
        jnp.dot(gate_grad, gate_full.T, preferred_element_type=jnp.float32)
        + jnp.dot(up_grad, up_full.T, preferred_element_type=jnp.float32)
    ).astype(jnp.bfloat16)
    down_grad = ring_reduce_scatter(
        lax.dot_general(
            scaled, hidden, (((0,), (0,)), ((), ())), preferred_element_type=jnp.float32
        ).astype(jnp.bfloat16),
        "dp",
    )
    grad_w_down = down_grad[None]
    returned = (
        lax.all_to_all(
            x_grad.reshape(n_expert, capacity, model_width),
            "expert",
            split_axis=0,
            concat_axis=0,
            tiled=True,
        ),
        lax.all_to_all(
            prob_sum.astype(jnp.bfloat16).reshape(n_expert, capacity),
            "expert",
            split_axis=0,
            concat_axis=0,
            tiled=True,
        ),
    )
    grad_slots = returned[0].reshape(slot_count, model_width)
    prob_slots = returned[1].reshape(slot_count)
    picked = grad_slots[target].astype(jnp.float32).reshape(tok_count, top_count, model_width)
    grad_x = jnp.sum(picked, axis=1).astype(jnp.bfloat16)
    grad_probs = prob_slots[target].reshape(tok_count, top_count)
    return (grad_x, grad_probs, grad_w_down)


def solution(mesh):
    return jax.shard_map(
        per_device,
        mesh=mesh,
        in_specs=(
            P(("dp", "expert"), None),
            P(("dp", "expert"), None),
            P(("dp", "expert"), None),
            P(("dp", "expert"), None),
            P("expert", "dp", None),
            P("expert", "dp", None),
            P("expert", "dp", None),
        ),
        out_specs=(P(("dp", "expert"), None), P(("dp", "expert"), None), P("expert", "dp", None)),
        check_vma=False,
    )
```

```python
import jax
import jax.numpy as jnp
from jax import lax
from jax.sharding import PartitionSpec as P


def ring_gather_rotated(shard, axis):
    n = lax.axis_size(axis)
    fwd = [(m, (m + 1) % n) for m in range(n)]
    bwd = [(m, (m - 1) % n) for m in range(n)]
    nf = n // 2
    nb = (n - 1) // 2
    f = shard
    b = shard
    got_f = {}
    got_b = {}
    for s in range(1, nf + 1):
        f = lax.ppermute(f, axis, fwd)
        got_f[s] = f
        if s <= nb:
            b = lax.ppermute(b, axis, bwd)
            got_b[s] = b
    pieces = [shard] + [got_b[k] for k in range(1, nb + 1)] + [got_f[n - k] for k in range(nb + 1, n)]
    return jnp.concatenate(pieces, axis=1)


def roll_cols(a, shift, width):
    doubled = jnp.concatenate([a, a], axis=1)
    return lax.dynamic_slice_in_dim(doubled, shift % width, width, axis=1)


def per_device(x_tokens, grad_out, expert_ids, route_probs, w_gate, w_up, w_down):
    tok_count, model_width = x_tokens.shape
    top_count = expert_ids.shape[1]
    n_expert = lax.axis_size("expert")
    capacity = tok_count * top_count * 5 // (4 * n_expert)
    slot_count = n_expert * capacity
    routes = tok_count * top_count
    flat_ids = expert_ids.reshape(routes)
    onehot = (flat_ids[:, None] == jnp.arange(n_expert, dtype=jnp.int32)).astype(jnp.int32)
    route_rank = jnp.sum((jnp.cumsum(onehot, axis=0) - onehot) * onehot, axis=1)
    target = flat_ids * capacity + route_rank
    source = (
        jnp.full((slot_count,), routes, jnp.int32)
        .at[target]
        .set(jnp.arange(routes, dtype=jnp.int32))
    )
    token_of = jnp.where(source < routes, source // top_count, tok_count)
    x_padded = jnp.concatenate([x_tokens, jnp.zeros((1, model_width), jnp.bfloat16)], axis=0)
    dy_padded = jnp.concatenate([grad_out, jnp.zeros((1, model_width), jnp.bfloat16)], axis=0)
    p_padded = jnp.concatenate([route_probs.reshape(routes), jnp.zeros((1,), jnp.float32)]).astype(
        jnp.bfloat16
    )
    x_slots = x_padded[token_of].reshape(n_expert, capacity, model_width)
    dy_slots = dy_padded[token_of].reshape(n_expert, capacity, model_width)
    p_slots = p_padded[source].reshape(n_expert, capacity)
    arrived = (
        lax.all_to_all(x_slots, "expert", split_axis=0, concat_axis=0, tiled=True),
        lax.all_to_all(dy_slots, "expert", split_axis=0, concat_axis=0, tiled=True),
        lax.all_to_all(p_slots, "expert", split_axis=0, concat_axis=0, tiled=True),
    )
    in_rows = arrived[0].reshape(slot_count, model_width)
    dy_rows = arrived[1].reshape(slot_count, model_width)
    p_rows = arrived[2].reshape(slot_count).astype(jnp.float32)
    scaled = (p_rows[:, None] * dy_rows.astype(jnp.float32)).astype(jnp.bfloat16)
    dp_index = lax.axis_index("dp")
    shard_rows = w_gate.shape[1]
    gu_rot = ring_gather_rotated(jnp.stack([w_gate[0], w_up[0]]), "dp")
    gate_full = gu_rot[0]
    up_full = gu_rot[1]
    in_rot = roll_cols(in_rows, dp_index * shard_rows, model_width)
    gate_pre = jnp.dot(in_rot, gate_full, preferred_element_type=jnp.float32)
    up_pre = jnp.dot(in_rot, up_full, preferred_element_type=jnp.float32)
    gate_sig = jax.nn.sigmoid(gate_pre)
    gate_act = gate_pre * gate_sig
    hidden = (gate_act * up_pre).astype(jnp.bfloat16)
    piece_rows = lax.all_gather(w_down, "dp", axis=1, tiled=True)[0]
    out_piece = jnp.dot(hidden, piece_rows.T, preferred_element_type=jnp.float32)
    grad_sum = jnp.dot(scaled, piece_rows, preferred_element_type=jnp.float32)
    prob_sum = jnp.sum(dy_rows.astype(jnp.float32) * out_piece, axis=1)
    hidden_grad, prob_sum = (grad_sum, prob_sum)
    up_grad = (hidden_grad * gate_act).astype(jnp.bfloat16)
    gate_grad = (hidden_grad * up_pre * gate_sig * (1.0 + gate_pre * (1.0 - gate_sig))).astype(
        jnp.bfloat16
    )
    x_grad_rot = (
        jnp.dot(gate_grad, gate_full.T, preferred_element_type=jnp.float32)
        + jnp.dot(up_grad, up_full.T, preferred_element_type=jnp.float32)
    ).astype(jnp.bfloat16)
    x_grad = roll_cols(x_grad_rot, -dp_index * shard_rows, model_width)
    down_grad = lax.psum_scatter(
        lax.dot_general(
            scaled, hidden, (((0,), (0,)), ((), ())), preferred_element_type=jnp.float32
        ).astype(jnp.bfloat16),
        "dp",
        scatter_dimension=0,
        tiled=True,
    )
    grad_w_down = down_grad[None]
    returned = (
        lax.all_to_all(
            x_grad.reshape(n_expert, capacity, model_width),
            "expert",
            split_axis=0,
            concat_axis=0,
            tiled=True,
        ),
        lax.all_to_all(
            prob_sum.astype(jnp.bfloat16).reshape(n_expert, capacity),
            "expert",
            split_axis=0,
            concat_axis=0,
            tiled=True,
        ),
    )
    grad_slots = returned[0].reshape(slot_count, model_width)
    prob_slots = returned[1].reshape(slot_count)
    picked = grad_slots[target].astype(jnp.float32).reshape(tok_count, top_count, model_width)
    grad_x = jnp.sum(picked, axis=1).astype(jnp.bfloat16)
    grad_probs = prob_slots[target].reshape(tok_count, top_count)
    return (grad_x, grad_probs, grad_w_down)


def solution(mesh):
    return jax.shard_map(
        per_device,
        mesh=mesh,
        in_specs=(
            P(("dp", "expert"), None),
            P(("dp", "expert"), None),
            P(("dp", "expert"), None),
            P(("dp", "expert"), None),
            P("expert", "dp", None),
            P("expert", "dp", None),
            P("expert", "dp", None),
        ),
        out_specs=(P(("dp", "expert"), None), P(("dp", "expert"), None), P("expert", "dp", None)),
        check_vma=False,
    )
```

```python
import jax
import jax.numpy as jnp
from jax import lax
from jax.sharding import PartitionSpec as P


def ring_gather_pieces(shard, axis):
    n = lax.axis_size(axis)
    fwd = [(m, (m + 1) % n) for m in range(n)]
    bwd = [(m, (m - 1) % n) for m in range(n)]
    nf = n // 2
    nb = (n - 1) // 2
    f = shard
    b = shard
    got_f = {}
    got_b = {}
    for s in range(1, nf + 1):
        f = lax.ppermute(f, axis, fwd)
        got_f[s] = f
        if s <= nb:
            b = lax.ppermute(b, axis, bwd)
            got_b[s] = b
    return [shard] + [got_b[k] for k in range(1, nb + 1)] + [got_f[n - k] for k in range(nb + 1, n)]


def roll_cols(a, shift, width):
    doubled = jnp.concatenate([a, a], axis=1)
    return lax.dynamic_slice_in_dim(doubled, shift % width, width, axis=1)


def per_device(x_tokens, grad_out, expert_ids, route_probs, w_gate, w_up, w_down):
    tok_count, model_width = x_tokens.shape
    top_count = expert_ids.shape[1]
    n_expert = lax.axis_size("expert")
    n_dp = lax.axis_size("dp")
    capacity = tok_count * top_count * 5 // (4 * n_expert)
    slot_count = n_expert * capacity
    routes = tok_count * top_count
    flat_ids = expert_ids.reshape(routes)
    onehot = (flat_ids[:, None] == jnp.arange(n_expert, dtype=jnp.int32)).astype(jnp.int32)
    route_rank = jnp.sum((jnp.cumsum(onehot, axis=0) - onehot) * onehot, axis=1)
    target = flat_ids * capacity + route_rank
    source = (
        jnp.full((slot_count,), routes, jnp.int32)
        .at[target]
        .set(jnp.arange(routes, dtype=jnp.int32))
    )
    token_of = jnp.where(source < routes, source // top_count, tok_count)
    lane = 128
    p_col = jnp.concatenate([route_probs.reshape(routes), jnp.zeros((1,), jnp.float32)]).astype(
        jnp.bfloat16
    )[source]
    p_block = jnp.zeros((slot_count, lane), jnp.bfloat16).at[:, 0].set(p_col)
    x_padded = jnp.concatenate([x_tokens, jnp.zeros((1, model_width), jnp.bfloat16)], axis=0)
    dy_padded = jnp.concatenate([grad_out, jnp.zeros((1, model_width), jnp.bfloat16)], axis=0)
    packed = jnp.concatenate([x_padded[token_of], dy_padded[token_of], p_block], axis=1)
    arrived = lax.all_to_all(
        packed.reshape(n_expert, capacity, 2 * model_width + lane),
        "expert",
        split_axis=0,
        concat_axis=0,
        tiled=True,
    ).reshape(slot_count, 2 * model_width + lane)
    in_rows = arrived[:, :model_width]
    dy_rows = arrived[:, model_width : 2 * model_width]
    p_rows = arrived[:, 2 * model_width].astype(jnp.float32)
    scaled = (p_rows[:, None] * dy_rows.astype(jnp.float32)).astype(jnp.bfloat16)

    dp_index = lax.axis_index("dp")
    shard_rows = w_gate.shape[1]
    pieces = ring_gather_pieces(jnp.stack([w_gate[0], w_up[0]]), "dp")
    in_rot = roll_cols(in_rows, dp_index * shard_rows, model_width)
    gate_pre = None
    up_pre = None
    for k, piece in enumerate(pieces):
        cols = in_rot[:, k * shard_rows : (k + 1) * shard_rows]
        g = jnp.dot(cols, piece[0], preferred_element_type=jnp.float32)
        u = jnp.dot(cols, piece[1], preferred_element_type=jnp.float32)
        gate_pre = g if gate_pre is None else gate_pre + g
        up_pre = u if up_pre is None else up_pre + u
    gate_sig = jax.nn.sigmoid(gate_pre)
    gate_act = gate_pre * gate_sig
    hidden = (gate_act * up_pre).astype(jnp.bfloat16)
    down_grad = lax.psum_scatter(
        lax.dot_general(
            scaled, hidden, (((0,), (0,)), ((), ())), preferred_element_type=jnp.float32
        ).astype(jnp.bfloat16),
        "dp",
        scatter_dimension=0,
        tiled=True,
    )
    grad_w_down = down_grad[None]
    piece_rows = lax.all_gather(w_down, "dp", axis=1, tiled=True)[0]
    out_piece = jnp.dot(hidden, piece_rows.T, preferred_element_type=jnp.float32)
    hidden_grad = jnp.dot(scaled, piece_rows, preferred_element_type=jnp.float32)
    prob_sum = jnp.sum(dy_rows.astype(jnp.float32) * out_piece, axis=1)
    up_grad = (hidden_grad * gate_act).astype(jnp.bfloat16)
    gate_grad = (hidden_grad * up_pre * gate_sig * (1.0 + gate_pre * (1.0 - gate_sig))).astype(
        jnp.bfloat16
    )
    x_grad_rot = jnp.concatenate(
        [
            (
                jnp.dot(gate_grad, piece[0].T, preferred_element_type=jnp.float32)
                + jnp.dot(up_grad, piece[1].T, preferred_element_type=jnp.float32)
            ).astype(jnp.bfloat16)
            for piece in pieces
        ],
        axis=1,
    )
    x_grad = roll_cols(x_grad_rot, -dp_index * shard_rows, model_width)
    prob_block = jnp.zeros((slot_count, lane), jnp.bfloat16).at[:, 0].set(prob_sum.astype(jnp.bfloat16))
    returned = lax.all_to_all(
        jnp.concatenate([x_grad, prob_block], axis=1).reshape(n_expert, capacity, model_width + lane),
        "expert",
        split_axis=0,
        concat_axis=0,
        tiled=True,
    ).reshape(slot_count, model_width + lane)
    grad_slots = returned[:, :model_width]
    prob_slots = returned[:, model_width]
    picked = grad_slots[target].astype(jnp.float32).reshape(tok_count, top_count, model_width)
    grad_x = jnp.sum(picked, axis=1).astype(jnp.bfloat16)
    grad_probs = prob_slots[target].reshape(tok_count, top_count)
    return (grad_x, grad_probs, grad_w_down)


def solution(mesh):
    return jax.shard_map(
        per_device,
        mesh=mesh,
        in_specs=(
            P(("dp", "expert"), None),
            P(("dp", "expert"), None),
            P(("dp", "expert"), None),
            P(("dp", "expert"), None),
            P("expert", "dp", None),
            P("expert", "dp", None),
            P("expert", "dp", None),
        ),
        out_specs=(P(("dp", "expert"), None), P(("dp", "expert"), None), P("expert", "dp", None)),
        check_vma=False,
    )
```

```python
import jax
import jax.numpy as jnp
from jax import lax
from jax.sharding import PartitionSpec as P


def ring_gather_pieces(shard, axis):
    n = lax.axis_size(axis)
    fwd = [(m, (m + 1) % n) for m in range(n)]
    bwd = [(m, (m - 1) % n) for m in range(n)]
    nf = n // 2
    nb = (n - 1) // 2
    f = shard
    b = shard
    got_f = {}
    got_b = {}
    for s in range(1, nf + 1):
        f = lax.ppermute(f, axis, fwd)
        got_f[s] = f
        if s <= nb:
            b = lax.ppermute(b, axis, bwd)
            got_b[s] = b
    return [shard] + [got_b[k] for k in range(1, nb + 1)] + [got_f[n - k] for k in range(nb + 1, n)]


def roll_cols(a, shift, width):
    doubled = jnp.concatenate([a, a], axis=1)
    return lax.dynamic_slice_in_dim(doubled, shift % width, width, axis=1)


def per_device(x_tokens, grad_out, expert_ids, route_probs, w_gate, w_up, w_down):
    tok_count, model_width = x_tokens.shape
    top_count = expert_ids.shape[1]
    n_expert = lax.axis_size("expert")
    n_dp = lax.axis_size("dp")
    capacity = tok_count * top_count * 5 // (4 * n_expert)
    slot_count = n_expert * capacity
    routes = tok_count * top_count
    flat_ids = expert_ids.reshape(routes)
    onehot = (flat_ids[:, None] == jnp.arange(n_expert, dtype=jnp.int32)).astype(jnp.int32)
    route_rank = jnp.sum((jnp.cumsum(onehot, axis=0) - onehot) * onehot, axis=1)
    target = flat_ids * capacity + route_rank
    source = (
        jnp.full((slot_count,), routes, jnp.int32)
        .at[target]
        .set(jnp.arange(routes, dtype=jnp.int32))
    )
    token_of = jnp.where(source < routes, source // top_count, tok_count)
    lane = 128
    p_col = jnp.concatenate([route_probs.reshape(routes), jnp.zeros((1,), jnp.float32)]).astype(
        jnp.bfloat16
    )[source]
    p_block = jnp.zeros((slot_count, lane), jnp.bfloat16).at[:, 0].set(p_col)
    x_padded = jnp.concatenate([x_tokens, jnp.zeros((1, model_width), jnp.bfloat16)], axis=0)
    dy_padded = jnp.concatenate([grad_out, jnp.zeros((1, model_width), jnp.bfloat16)], axis=0)
    packed = jnp.concatenate([x_padded[token_of], dy_padded[token_of], p_block], axis=1)
    arrived = lax.all_to_all(
        packed.reshape(n_expert, capacity, 2 * model_width + lane),
        "expert",
        split_axis=0,
        concat_axis=0,
        tiled=True,
    ).reshape(slot_count, 2 * model_width + lane)
    in_rows = arrived[:, :model_width]
    dy_rows = arrived[:, model_width : 2 * model_width]
    p_rows = arrived[:, 2 * model_width].astype(jnp.float32)
    scaled = (p_rows[:, None] * dy_rows.astype(jnp.float32)).astype(jnp.bfloat16)

    dp_index = lax.axis_index("dp")
    shard_rows = w_gate.shape[1]
    pieces = ring_gather_pieces(jnp.stack([w_gate[0], w_up[0], w_down[0]]), "dp")
    in_rot = roll_cols(in_rows, dp_index * shard_rows, model_width)
    gate_pre = None
    up_pre = None
    for k, piece in enumerate(pieces):
        cols = in_rot[:, k * shard_rows : (k + 1) * shard_rows]
        g = jnp.dot(cols, piece[0], preferred_element_type=jnp.float32)
        u = jnp.dot(cols, piece[1], preferred_element_type=jnp.float32)
        gate_pre = g if gate_pre is None else gate_pre + g
        up_pre = u if up_pre is None else up_pre + u
    gate_sig = jax.nn.sigmoid(gate_pre)
    gate_act = gate_pre * gate_sig
    hidden = (gate_act * up_pre).astype(jnp.bfloat16)
    down_grad = lax.psum_scatter(
        lax.dot_general(
            scaled, hidden, (((0,), (0,)), ((), ())), preferred_element_type=jnp.float32
        ).astype(jnp.bfloat16),
        "dp",
        scatter_dimension=0,
        tiled=True,
    )
    grad_w_down = down_grad[None]
    dy_rot = roll_cols(dy_rows, dp_index * shard_rows, model_width)
    scaled_rot = (p_rows[:, None] * dy_rot.astype(jnp.float32)).astype(jnp.bfloat16)
    hidden_grad = None
    prob_sum = None
    for k, piece in enumerate(pieces):
        block = slice(k * shard_rows, (k + 1) * shard_rows)
        out_piece = jnp.dot(hidden, piece[2].T, preferred_element_type=jnp.float32)
        prob_k = jnp.sum(dy_rot[:, block].astype(jnp.float32) * out_piece, axis=1)
        grad_k = jnp.dot(scaled_rot[:, block], piece[2], preferred_element_type=jnp.float32)
        prob_sum = prob_k if prob_sum is None else prob_sum + prob_k
        hidden_grad = grad_k if hidden_grad is None else hidden_grad + grad_k
    up_grad = (hidden_grad * gate_act).astype(jnp.bfloat16)
    gate_grad = (hidden_grad * up_pre * gate_sig * (1.0 + gate_pre * (1.0 - gate_sig))).astype(
        jnp.bfloat16
    )
    x_grad_rot = jnp.concatenate(
        [
            (
                jnp.dot(gate_grad, piece[0].T, preferred_element_type=jnp.float32)
                + jnp.dot(up_grad, piece[1].T, preferred_element_type=jnp.float32)
            ).astype(jnp.bfloat16)
            for piece in pieces
        ],
        axis=1,
    )
    x_grad = roll_cols(x_grad_rot, -dp_index * shard_rows, model_width)
    prob_block = jnp.zeros((slot_count, lane), jnp.bfloat16).at[:, 0].set(prob_sum.astype(jnp.bfloat16))
    returned = lax.all_to_all(
        jnp.concatenate([x_grad, prob_block], axis=1).reshape(n_expert, capacity, model_width + lane),
        "expert",
        split_axis=0,
        concat_axis=0,
        tiled=True,
    ).reshape(slot_count, model_width + lane)
    grad_slots = returned[:, :model_width]
    prob_slots = returned[:, model_width]
    picked = grad_slots[target].astype(jnp.float32).reshape(tok_count, top_count, model_width)
    grad_x = jnp.sum(picked, axis=1).astype(jnp.bfloat16)
    grad_probs = prob_slots[target].reshape(tok_count, top_count)
    return (grad_x, grad_probs, grad_w_down)


def solution(mesh):
    return jax.shard_map(
        per_device,
        mesh=mesh,
        in_specs=(
            P(("dp", "expert"), None),
            P(("dp", "expert"), None),
            P(("dp", "expert"), None),
            P(("dp", "expert"), None),
            P("expert", "dp", None),
            P("expert", "dp", None),
            P("expert", "dp", None),
        ),
        out_specs=(P(("dp", "expert"), None), P(("dp", "expert"), None), P("expert", "dp", None)),
        check_vma=False,
    )
```

```python
import jax
import jax.numpy as jnp
from jax import lax
from jax.sharding import PartitionSpec as P


def ring_gather_pieces(shard, axis):
    n = lax.axis_size(axis)
    fwd = [(m, (m + 1) % n) for m in range(n)]
    bwd = [(m, (m - 1) % n) for m in range(n)]
    nf = n // 2
    nb = (n - 1) // 2
    f = shard
    b = shard
    got_f = {}
    got_b = {}
    for s in range(1, nf + 1):
        f = lax.ppermute(f, axis, fwd)
        got_f[s] = f
        if s <= nb:
            b = lax.ppermute(b, axis, bwd)
            got_b[s] = b
    return [shard] + [got_b[k] for k in range(1, nb + 1)] + [got_f[n - k] for k in range(nb + 1, n)]


def roll_cols(a, shift, width):
    doubled = jnp.concatenate([a, a], axis=1)
    return lax.dynamic_slice_in_dim(doubled, shift % width, width, axis=1)


def per_device(x_tokens, grad_out, expert_ids, route_probs, w_gate, w_up, w_down):
    tok_count, model_width = x_tokens.shape
    top_count = expert_ids.shape[1]
    n_expert = lax.axis_size("expert")
    n_dp = lax.axis_size("dp")
    capacity = tok_count * top_count * 5 // (4 * n_expert)
    slot_count = n_expert * capacity
    routes = tok_count * top_count
    flat_ids = expert_ids.reshape(routes)
    onehot = (flat_ids[:, None] == jnp.arange(n_expert, dtype=jnp.int32)).astype(jnp.int32)
    route_rank = jnp.sum((jnp.cumsum(onehot, axis=0) - onehot) * onehot, axis=1)
    target = flat_ids * capacity + route_rank
    source = (
        jnp.full((slot_count,), routes, jnp.int32)
        .at[target]
        .set(jnp.arange(routes, dtype=jnp.int32))
    )
    token_of = jnp.where(source < routes, source // top_count, tok_count)
    lane = 128
    p_col = jnp.concatenate([route_probs.reshape(routes), jnp.zeros((1,), jnp.float32)]).astype(
        jnp.bfloat16
    )[source]
    p_block = jnp.zeros((slot_count, lane), jnp.bfloat16).at[:, 0].set(p_col)
    x_padded = jnp.concatenate([x_tokens, jnp.zeros((1, model_width), jnp.bfloat16)], axis=0)
    dy_padded = jnp.concatenate([grad_out, jnp.zeros((1, model_width), jnp.bfloat16)], axis=0)
    packed = jnp.concatenate([x_padded[token_of], dy_padded[token_of], p_block], axis=1)
    dp_index = lax.axis_index("dp")
    shard_rows = w_gate.shape[1]
    pieces = ring_gather_pieces(jnp.stack([w_gate[0], w_up[0]]), "dp")
    packed, _ = lax.optimization_barrier((packed, pieces[-1]))
    arrived = lax.all_to_all(
        packed.reshape(n_expert, capacity, 2 * model_width + lane),
        "expert",
        split_axis=0,
        concat_axis=0,
        tiled=True,
    ).reshape(slot_count, 2 * model_width + lane)
    in_rows = arrived[:, :model_width]
    dy_rows = arrived[:, model_width : 2 * model_width]
    p_rows = arrived[:, 2 * model_width].astype(jnp.float32)
    scaled = (p_rows[:, None] * dy_rows.astype(jnp.float32)).astype(jnp.bfloat16)

    in_rot = roll_cols(in_rows, dp_index * shard_rows, model_width)
    gate_pre = None
    up_pre = None
    for k, piece in enumerate(pieces):
        cols = in_rot[:, k * shard_rows : (k + 1) * shard_rows]
        g = jnp.dot(cols, piece[0], preferred_element_type=jnp.float32)
        u = jnp.dot(cols, piece[1], preferred_element_type=jnp.float32)
        gate_pre = g if gate_pre is None else gate_pre + g
        up_pre = u if up_pre is None else up_pre + u
    gate_sig = jax.nn.sigmoid(gate_pre)
    gate_act = gate_pre * gate_sig
    hidden = (gate_act * up_pre).astype(jnp.bfloat16)
    down_grad = lax.psum_scatter(
        lax.dot_general(
            scaled, hidden, (((0,), (0,)), ((), ())), preferred_element_type=jnp.float32
        ).astype(jnp.bfloat16),
        "dp",
        scatter_dimension=0,
        tiled=True,
    )
    grad_w_down = down_grad[None]
    piece_rows = lax.all_gather(w_down, "dp", axis=1, tiled=True)[0]
    out_piece = jnp.dot(hidden, piece_rows.T, preferred_element_type=jnp.float32)
    hidden_grad = jnp.dot(scaled, piece_rows, preferred_element_type=jnp.float32)
    prob_sum = jnp.sum(dy_rows.astype(jnp.float32) * out_piece, axis=1)
    up_grad = (hidden_grad * gate_act).astype(jnp.bfloat16)
    gate_grad = (hidden_grad * up_pre * gate_sig * (1.0 + gate_pre * (1.0 - gate_sig))).astype(
        jnp.bfloat16
    )
    x_grad_rot = jnp.concatenate(
        [
            (
                jnp.dot(gate_grad, piece[0].T, preferred_element_type=jnp.float32)
                + jnp.dot(up_grad, piece[1].T, preferred_element_type=jnp.float32)
            ).astype(jnp.bfloat16)
            for piece in pieces
        ],
        axis=1,
    )
    x_grad = roll_cols(x_grad_rot, -dp_index * shard_rows, model_width)
    prob_block = jnp.zeros((slot_count, lane), jnp.bfloat16).at[:, 0].set(prob_sum.astype(jnp.bfloat16))
    returned = lax.all_to_all(
        jnp.concatenate([x_grad, prob_block], axis=1).reshape(n_expert, capacity, model_width + lane),
        "expert",
        split_axis=0,
        concat_axis=0,
        tiled=True,
    ).reshape(slot_count, model_width + lane)
    grad_slots = returned[:, :model_width]
    prob_slots = returned[:, model_width]
    picked = grad_slots[target].astype(jnp.float32).reshape(tok_count, top_count, model_width)
    grad_x = jnp.sum(picked, axis=1).astype(jnp.bfloat16)
    grad_probs = prob_slots[target].reshape(tok_count, top_count)
    return (grad_x, grad_probs, grad_w_down)


def solution(mesh):
    return jax.shard_map(
        per_device,
        mesh=mesh,
        in_specs=(
            P(("dp", "expert"), None),
            P(("dp", "expert"), None),
            P(("dp", "expert"), None),
            P(("dp", "expert"), None),
            P("expert", "dp", None),
            P("expert", "dp", None),
            P("expert", "dp", None),
        ),
        out_specs=(P(("dp", "expert"), None), P(("dp", "expert"), None), P("expert", "dp", None)),
        check_vma=False,
    )
```

```python
import jax
import jax.numpy as jnp
from jax import lax
from jax.sharding import PartitionSpec as P


def ring_gather_pieces(shard, axis):
    n = lax.axis_size(axis)
    fwd = [(m, (m + 1) % n) for m in range(n)]
    bwd = [(m, (m - 1) % n) for m in range(n)]
    nf = n // 2
    nb = (n - 1) // 2
    f = shard
    b = shard
    got_f = {}
    got_b = {}
    for s in range(1, nf + 1):
        f = lax.ppermute(f, axis, fwd)
        got_f[s] = f
        if s <= nb:
            b = lax.ppermute(b, axis, bwd)
            got_b[s] = b
    return [shard] + [got_b[k] for k in range(1, nb + 1)] + [got_f[n - k] for k in range(nb + 1, n)]


def roll_cols(a, shift, width):
    doubled = jnp.concatenate([a, a], axis=1)
    return lax.dynamic_slice_in_dim(doubled, shift % width, width, axis=1)


def per_device(x_tokens, grad_out, expert_ids, route_probs, w_gate, w_up, w_down):
    tok_count, model_width = x_tokens.shape
    top_count = expert_ids.shape[1]
    n_expert = lax.axis_size("expert")
    n_dp = lax.axis_size("dp")
    capacity = tok_count * top_count * 5 // (4 * n_expert)
    slot_count = n_expert * capacity
    routes = tok_count * top_count
    flat_ids = expert_ids.reshape(routes)
    onehot = (flat_ids[:, None] == jnp.arange(n_expert, dtype=jnp.int32)).astype(jnp.int32)
    route_rank = jnp.sum((jnp.cumsum(onehot, axis=0) - onehot) * onehot, axis=1)
    target = flat_ids * capacity + route_rank
    source = (
        jnp.full((slot_count,), routes, jnp.int32)
        .at[target]
        .set(jnp.arange(routes, dtype=jnp.int32))
    )
    token_of = jnp.where(source < routes, source // top_count, tok_count)
    lane = 128
    p_col = jnp.concatenate([route_probs.reshape(routes), jnp.zeros((1,), jnp.float32)]).astype(
        jnp.bfloat16
    )[source]
    p_block = jnp.zeros((slot_count, lane), jnp.bfloat16).at[:, 0].set(p_col)
    x_padded = jnp.concatenate([x_tokens, jnp.zeros((1, model_width), jnp.bfloat16)], axis=0)
    dy_padded = jnp.concatenate([grad_out, jnp.zeros((1, model_width), jnp.bfloat16)], axis=0)
    packed = jnp.concatenate([x_padded[token_of], dy_padded[token_of], p_block], axis=1)
    dp_index = lax.axis_index("dp")
    shard_rows = w_gate.shape[1]
    pieces = ring_gather_pieces(jnp.stack([w_gate[0], w_up[0]]), "dp")
    packed, _, _ = lax.optimization_barrier((packed, pieces[1], pieces[-1]))
    arrived = lax.all_to_all(
        packed.reshape(n_expert, capacity, 2 * model_width + lane),
        "expert",
        split_axis=0,
        concat_axis=0,
        tiled=True,
    ).reshape(slot_count, 2 * model_width + lane)
    in_rows = arrived[:, :model_width]
    dy_rows = arrived[:, model_width : 2 * model_width]
    p_rows = arrived[:, 2 * model_width].astype(jnp.float32)
    scaled = (p_rows[:, None] * dy_rows.astype(jnp.float32)).astype(jnp.bfloat16)

    in_rot = roll_cols(in_rows, dp_index * shard_rows, model_width)
    gate_pre = None
    up_pre = None
    for k, piece in enumerate(pieces):
        cols = in_rot[:, k * shard_rows : (k + 1) * shard_rows]
        g = jnp.dot(cols, piece[0], preferred_element_type=jnp.float32)
        u = jnp.dot(cols, piece[1], preferred_element_type=jnp.float32)
        gate_pre = g if gate_pre is None else gate_pre + g
        up_pre = u if up_pre is None else up_pre + u
    gate_sig = jax.nn.sigmoid(gate_pre)
    gate_act = gate_pre * gate_sig
    hidden = (gate_act * up_pre).astype(jnp.bfloat16)
    down_grad = lax.psum_scatter(
        lax.dot_general(
            scaled, hidden, (((0,), (0,)), ((), ())), preferred_element_type=jnp.float32
        ).astype(jnp.bfloat16),
        "dp",
        scatter_dimension=0,
        tiled=True,
    )
    grad_w_down = down_grad[None]
    piece_rows = lax.all_gather(w_down, "dp", axis=1, tiled=True)[0]
    out_piece = jnp.dot(hidden, piece_rows.T, preferred_element_type=jnp.float32)
    hidden_grad = jnp.dot(scaled, piece_rows, preferred_element_type=jnp.float32)
    prob_sum = jnp.sum(dy_rows.astype(jnp.float32) * out_piece, axis=1)
    up_grad = (hidden_grad * gate_act).astype(jnp.bfloat16)
    gate_grad = (hidden_grad * up_pre * gate_sig * (1.0 + gate_pre * (1.0 - gate_sig))).astype(
        jnp.bfloat16
    )
    x_grad_rot = jnp.concatenate(
        [
            (
                jnp.dot(gate_grad, piece[0].T, preferred_element_type=jnp.float32)
                + jnp.dot(up_grad, piece[1].T, preferred_element_type=jnp.float32)
            ).astype(jnp.bfloat16)
            for piece in pieces
        ],
        axis=1,
    )
    x_grad = roll_cols(x_grad_rot, -dp_index * shard_rows, model_width)
    prob_block = jnp.zeros((slot_count, lane), jnp.bfloat16).at[:, 0].set(prob_sum.astype(jnp.bfloat16))
    returned = lax.all_to_all(
        jnp.concatenate([x_grad, prob_block], axis=1).reshape(n_expert, capacity, model_width + lane),
        "expert",
        split_axis=0,
        concat_axis=0,
        tiled=True,
    ).reshape(slot_count, model_width + lane)
    grad_slots = returned[:, :model_width]
    prob_slots = returned[:, model_width]
    picked = grad_slots[target].astype(jnp.float32).reshape(tok_count, top_count, model_width)
    grad_x = jnp.sum(picked, axis=1).astype(jnp.bfloat16)
    grad_probs = prob_slots[target].reshape(tok_count, top_count)
    return (grad_x, grad_probs, grad_w_down)


def solution(mesh):
    return jax.shard_map(
        per_device,
        mesh=mesh,
        in_specs=(
            P(("dp", "expert"), None),
            P(("dp", "expert"), None),
            P(("dp", "expert"), None),
            P(("dp", "expert"), None),
            P("expert", "dp", None),
            P("expert", "dp", None),
            P("expert", "dp", None),
        ),
        out_specs=(P(("dp", "expert"), None), P(("dp", "expert"), None), P("expert", "dp", None)),
        check_vma=False,
    )
```

```python
import jax
import jax.numpy as jnp
from jax import lax
from jax.sharding import PartitionSpec as P


def ring_gather_pieces(shard, axis):
    n = lax.axis_size(axis)
    fwd = [(m, (m + 1) % n) for m in range(n)]
    bwd = [(m, (m - 1) % n) for m in range(n)]
    nf = n // 2
    nb = (n - 1) // 2
    f = shard
    b = shard
    got_f = {}
    got_b = {}
    for s in range(1, nf + 1):
        f = lax.ppermute(f, axis, fwd)
        got_f[s] = f
        if s <= nb:
            b = lax.ppermute(b, axis, bwd)
            got_b[s] = b
    return [shard] + [got_b[k] for k in range(1, nb + 1)] + [got_f[n - k] for k in range(nb + 1, n)]


def roll_cols(a, shift, width):
    doubled = jnp.concatenate([a, a], axis=1)
    return lax.dynamic_slice_in_dim(doubled, shift % width, width, axis=1)


def per_device(x_tokens, grad_out, expert_ids, route_probs, w_gate, w_up, w_down):
    tok_count, model_width = x_tokens.shape
    top_count = expert_ids.shape[1]
    n_expert = lax.axis_size("expert")
    n_dp = lax.axis_size("dp")
    capacity = tok_count * top_count * 5 // (4 * n_expert)
    slot_count = n_expert * capacity
    routes = tok_count * top_count
    flat_ids = expert_ids.reshape(routes)
    onehot = (flat_ids[:, None] == jnp.arange(n_expert, dtype=jnp.int32)).astype(jnp.int32)
    route_rank = jnp.sum((jnp.cumsum(onehot, axis=0) - onehot) * onehot, axis=1)
    target = flat_ids * capacity + route_rank
    source = (
        jnp.full((slot_count,), routes, jnp.int32)
        .at[target]
        .set(jnp.arange(routes, dtype=jnp.int32))
    )
    token_of = jnp.where(source < routes, source // top_count, tok_count)
    lane = 128
    p_col = jnp.concatenate([route_probs.reshape(routes), jnp.zeros((1,), jnp.float32)]).astype(
        jnp.bfloat16
    )[source]
    p_block = jnp.zeros((slot_count, lane), jnp.bfloat16).at[:, 0].set(p_col)
    x_padded = jnp.concatenate([x_tokens, jnp.zeros((1, model_width), jnp.bfloat16)], axis=0)
    dy_padded = jnp.concatenate([grad_out, jnp.zeros((1, model_width), jnp.bfloat16)], axis=0)
    packed = jnp.concatenate([x_padded[token_of], dy_padded[token_of], p_block], axis=1)
    arrived = lax.all_to_all(
        packed.reshape(n_expert, capacity, 2 * model_width + lane),
        "expert",
        split_axis=0,
        concat_axis=0,
        tiled=True,
    ).reshape(slot_count, 2 * model_width + lane)
    in_rows = arrived[:, :model_width]
    dy_rows = arrived[:, model_width : 2 * model_width]
    p_rows = arrived[:, 2 * model_width].astype(jnp.float32)
    scaled = (p_rows[:, None] * dy_rows.astype(jnp.float32)).astype(jnp.bfloat16)

    dp_index = lax.axis_index("dp")
    n_dp = lax.axis_size("dp")
    shard_rows = w_gate.shape[1]
    half = w_gate.shape[2] // 2
    in_rot = roll_cols(in_rows, dp_index * shard_rows, model_width)
    shard_a = jnp.stack([w_gate[0][:, :half], w_up[0][:, :half]])
    shard_b = jnp.stack([w_gate[0][:, half:], w_up[0][:, half:]])
    pieces_a = ring_gather_pieces(shard_a, "dp")
    piece_rows = lax.all_gather(w_down, "dp", axis=1, tiled=True)[0]

    def half_hidden(pieces):
        gate_pre = None
        up_pre = None
        for k, piece in enumerate(pieces):
            cols = in_rot[:, k * shard_rows : (k + 1) * shard_rows]
            g = jnp.dot(cols, piece[0], preferred_element_type=jnp.float32)
            u = jnp.dot(cols, piece[1], preferred_element_type=jnp.float32)
            gate_pre = g if gate_pre is None else gate_pre + g
            up_pre = u if up_pre is None else up_pre + u
        gate_sig = jax.nn.sigmoid(gate_pre)
        gate_act = gate_pre * gate_sig
        hidden = (gate_act * up_pre).astype(jnp.bfloat16)
        partial = lax.dot_general(
            scaled, hidden, (((0,), (0,)), ((), ())), preferred_element_type=jnp.float32
        ).astype(jnp.bfloat16)
        return gate_pre, up_pre, gate_sig, gate_act, hidden, partial

    def half_backward(pieces, fwd, cols_down):
        gate_pre, up_pre, gate_sig, gate_act, hidden, _ = fwd
        out_piece = jnp.dot(hidden, cols_down.T, preferred_element_type=jnp.float32)
        hidden_grad = jnp.dot(scaled, cols_down, preferred_element_type=jnp.float32)
        up_grad = (hidden_grad * gate_act).astype(jnp.bfloat16)
        gate_grad = (hidden_grad * up_pre * gate_sig * (1.0 + gate_pre * (1.0 - gate_sig))).astype(
            jnp.bfloat16
        )
        x_parts = [
            jnp.dot(gate_grad, piece[0].T, preferred_element_type=jnp.float32)
            + jnp.dot(up_grad, piece[1].T, preferred_element_type=jnp.float32)
            for piece in pieces
        ]
        return out_piece, x_parts

    fwd_a = half_hidden(pieces_a)
    shard_b, partial_a = lax.optimization_barrier((shard_b, fwd_a[5]))
    down_a = lax.psum_scatter(partial_a, "dp", scatter_dimension=0, tiled=True)
    pieces_b = ring_gather_pieces(shard_b, "dp")
    fwd_b = half_hidden(pieces_b)
    down_b = lax.psum_scatter(fwd_b[5], "dp", scatter_dimension=0, tiled=True)
    out_a, x_parts_a = half_backward(pieces_a, fwd_a, piece_rows[:, :half])
    out_b, x_parts_b = half_backward(pieces_b, fwd_b, piece_rows[:, half:])
    grad_w_down = jnp.concatenate([down_a, down_b], axis=1)[None]
    prob_sum = jnp.sum(dy_rows.astype(jnp.float32) * (out_a + out_b), axis=1)
    x_grad_rot = jnp.concatenate(
        [(pa + pb).astype(jnp.bfloat16) for pa, pb in zip(x_parts_a, x_parts_b)], axis=1
    )
    x_grad = roll_cols(x_grad_rot, -dp_index * shard_rows, model_width)
    prob_block = jnp.zeros((slot_count, lane), jnp.bfloat16).at[:, 0].set(prob_sum.astype(jnp.bfloat16))
    returned = lax.all_to_all(
        jnp.concatenate([x_grad, prob_block], axis=1).reshape(n_expert, capacity, model_width + lane),
        "expert",
        split_axis=0,
        concat_axis=0,
        tiled=True,
    ).reshape(slot_count, model_width + lane)
    grad_slots = returned[:, :model_width]
    prob_slots = returned[:, model_width]
    picked = grad_slots[target].astype(jnp.float32).reshape(tok_count, top_count, model_width)
    grad_x = jnp.sum(picked, axis=1).astype(jnp.bfloat16)
    grad_probs = prob_slots[target].reshape(tok_count, top_count)
    return (grad_x, grad_probs, grad_w_down)


def solution(mesh):
    return jax.shard_map(
        per_device,
        mesh=mesh,
        in_specs=(
            P(("dp", "expert"), None),
            P(("dp", "expert"), None),
            P(("dp", "expert"), None),
            P(("dp", "expert"), None),
            P("expert", "dp", None),
            P("expert", "dp", None),
            P("expert", "dp", None),
        ),
        out_specs=(P(("dp", "expert"), None), P(("dp", "expert"), None), P("expert", "dp", None)),
        check_vma=False,
    )
```

```python
import jax
import jax.numpy as jnp
from jax import lax
from jax.sharding import PartitionSpec as P


def ring_gather_pieces(shard, axis):
    n = lax.axis_size(axis)
    fwd = [(m, (m + 1) % n) for m in range(n)]
    bwd = [(m, (m - 1) % n) for m in range(n)]
    nf = n // 2
    nb = (n - 1) // 2
    f = shard
    b = shard
    got_f = {}
    got_b = {}
    for s in range(1, nf + 1):
        f = lax.ppermute(f, axis, fwd)
        got_f[s] = f
        if s <= nb:
            b = lax.ppermute(b, axis, bwd)
            got_b[s] = b
    return [shard] + [got_b[k] for k in range(1, nb + 1)] + [got_f[n - k] for k in range(nb + 1, n)]


def roll_cols(a, shift, width):
    doubled = jnp.concatenate([a, a], axis=1)
    return lax.dynamic_slice_in_dim(doubled, shift % width, width, axis=1)


def per_device(x_tokens, grad_out, expert_ids, route_probs, w_gate, w_up, w_down):
    tok_count, model_width = x_tokens.shape
    top_count = expert_ids.shape[1]
    n_expert = lax.axis_size("expert")
    n_dp = lax.axis_size("dp")
    capacity = tok_count * top_count * 5 // (4 * n_expert)
    slot_count = n_expert * capacity
    routes = tok_count * top_count
    flat_ids = expert_ids.reshape(routes)
    onehot = (flat_ids[:, None] == jnp.arange(n_expert, dtype=jnp.int32)).astype(jnp.int32)
    route_rank = jnp.sum((jnp.cumsum(onehot, axis=0) - onehot) * onehot, axis=1)
    target = flat_ids * capacity + route_rank
    source = (
        jnp.full((slot_count,), routes, jnp.int32)
        .at[target]
        .set(jnp.arange(routes, dtype=jnp.int32))
    )
    token_of = jnp.where(source < routes, source // top_count, tok_count)
    lane = 128
    p_col = jnp.concatenate([route_probs.reshape(routes), jnp.zeros((1,), jnp.float32)]).astype(
        jnp.bfloat16
    )[source]
    p_block = jnp.zeros((slot_count, lane), jnp.bfloat16).at[:, 0].set(p_col)
    x_padded = jnp.concatenate([x_tokens, jnp.zeros((1, model_width), jnp.bfloat16)], axis=0)
    dy_padded = jnp.concatenate([grad_out, jnp.zeros((1, model_width), jnp.bfloat16)], axis=0)
    packed = jnp.concatenate([x_padded[token_of], dy_padded[token_of], p_block], axis=1)
    dp_index = lax.axis_index("dp")
    shard_rows = w_gate.shape[1]
    pieces = ring_gather_pieces(jnp.stack([w_gate[0], w_up[0]]), "dp")
    packed, _ = lax.optimization_barrier((packed, pieces[-1]))
    arrived = lax.all_to_all(
        packed.reshape(n_expert, capacity, 2 * model_width + lane),
        "expert",
        split_axis=0,
        concat_axis=0,
        tiled=True,
    ).reshape(slot_count, 2 * model_width + lane)
    in_rows = arrived[:, :model_width]
    dy_rows = arrived[:, model_width : 2 * model_width]
    p_rows = arrived[:, 2 * model_width].astype(jnp.float32)
    scaled = (p_rows[:, None] * dy_rows.astype(jnp.float32)).astype(jnp.bfloat16)

    in_rot = roll_cols(in_rows, dp_index * shard_rows, model_width)
    paired = [
        jnp.concatenate(pieces[k : k + 2], axis=1) for k in range(0, len(pieces) - 1, 2)
    ] + ([pieces[-1]] if len(pieces) % 2 else [])
    pair_rows = [p.shape[1] for p in paired]
    pair_start = [sum(pair_rows[:j]) for j in range(len(paired))]
    gate_pre = None
    up_pre = None
    for piece, lo, width in zip(paired, pair_start, pair_rows):
        cols = in_rot[:, lo : lo + width]
        g = jnp.dot(cols, piece[0], preferred_element_type=jnp.float32)
        u = jnp.dot(cols, piece[1], preferred_element_type=jnp.float32)
        gate_pre = g if gate_pre is None else gate_pre + g
        up_pre = u if up_pre is None else up_pre + u
    gate_sig = jax.nn.sigmoid(gate_pre)
    gate_act = gate_pre * gate_sig
    hidden = (gate_act * up_pre).astype(jnp.bfloat16)
    down_grad = lax.psum_scatter(
        lax.dot_general(
            scaled, hidden, (((0,), (0,)), ((), ())), preferred_element_type=jnp.float32
        ).astype(jnp.bfloat16),
        "dp",
        scatter_dimension=0,
        tiled=True,
    )
    grad_w_down = down_grad[None]
    piece_rows = lax.all_gather(w_down, "dp", axis=1, tiled=True)[0]
    out_piece = jnp.dot(hidden, piece_rows.T, preferred_element_type=jnp.float32)
    hidden_grad = jnp.dot(scaled, piece_rows, preferred_element_type=jnp.float32)
    prob_sum = jnp.sum(dy_rows.astype(jnp.float32) * out_piece, axis=1)
    up_grad = (hidden_grad * gate_act).astype(jnp.bfloat16)
    gate_grad = (hidden_grad * up_pre * gate_sig * (1.0 + gate_pre * (1.0 - gate_sig))).astype(
        jnp.bfloat16
    )
    x_grad_rot = jnp.concatenate(
        [
            (
                jnp.dot(gate_grad, piece[0].T, preferred_element_type=jnp.float32)
                + jnp.dot(up_grad, piece[1].T, preferred_element_type=jnp.float32)
            ).astype(jnp.bfloat16)
            for piece in paired
        ],
        axis=1,
    )
    x_grad = roll_cols(x_grad_rot, -dp_index * shard_rows, model_width)
    prob_block = jnp.zeros((slot_count, lane), jnp.bfloat16).at[:, 0].set(prob_sum.astype(jnp.bfloat16))
    returned = lax.all_to_all(
        jnp.concatenate([x_grad, prob_block], axis=1).reshape(n_expert, capacity, model_width + lane),
        "expert",
        split_axis=0,
        concat_axis=0,
        tiled=True,
    ).reshape(slot_count, model_width + lane)
    grad_slots = returned[:, :model_width]
    prob_slots = returned[:, model_width]
    picked = grad_slots[target].astype(jnp.float32).reshape(tok_count, top_count, model_width)
    grad_x = jnp.sum(picked, axis=1).astype(jnp.bfloat16)
    grad_probs = prob_slots[target].reshape(tok_count, top_count)
    return (grad_x, grad_probs, grad_w_down)


def solution(mesh):
    return jax.shard_map(
        per_device,
        mesh=mesh,
        in_specs=(
            P(("dp", "expert"), None),
            P(("dp", "expert"), None),
            P(("dp", "expert"), None),
            P(("dp", "expert"), None),
            P("expert", "dp", None),
            P("expert", "dp", None),
            P("expert", "dp", None),
        ),
        out_specs=(P(("dp", "expert"), None), P(("dp", "expert"), None), P("expert", "dp", None)),
        check_vma=False,
    )
```

```python
import jax
import jax.numpy as jnp
from jax import lax
from jax.sharding import PartitionSpec as P


def ring_gather_pieces(shard, axis):
    n = lax.axis_size(axis)
    fwd = [(m, (m + 1) % n) for m in range(n)]
    bwd = [(m, (m - 1) % n) for m in range(n)]
    nf = n // 2
    nb = (n - 1) // 2
    f = shard
    b = shard
    got_f = {}
    got_b = {}
    for s in range(1, nf + 1):
        f = lax.ppermute(f, axis, fwd)
        got_f[s] = f
        if s <= nb:
            b = lax.ppermute(b, axis, bwd)
            got_b[s] = b
    return [shard] + [got_b[k] for k in range(1, nb + 1)] + [got_f[n - k] for k in range(nb + 1, n)]


def roll_cols(a, shift, width):
    doubled = jnp.concatenate([a, a], axis=1)
    return lax.dynamic_slice_in_dim(doubled, shift % width, width, axis=1)


def per_device(x_tokens, grad_out, expert_ids, route_probs, w_gate, w_up, w_down):
    tok_count, model_width = x_tokens.shape
    top_count = expert_ids.shape[1]
    n_expert = lax.axis_size("expert")
    n_dp = lax.axis_size("dp")
    capacity = tok_count * top_count * 5 // (4 * n_expert)
    slot_count = n_expert * capacity
    routes = tok_count * top_count
    flat_ids = expert_ids.reshape(routes)
    onehot = (flat_ids[:, None] == jnp.arange(n_expert, dtype=jnp.int32)).astype(jnp.int32)
    route_rank = jnp.sum((jnp.cumsum(onehot, axis=0) - onehot) * onehot, axis=1)
    target = flat_ids * capacity + route_rank
    source = (
        jnp.full((slot_count,), routes, jnp.int32)
        .at[target]
        .set(jnp.arange(routes, dtype=jnp.int32))
    )
    token_of = jnp.where(source < routes, source // top_count, tok_count)
    lane = 128
    p_col = jnp.concatenate([route_probs.reshape(routes), jnp.zeros((1,), jnp.float32)]).astype(
        jnp.bfloat16
    )[source]
    p_block = jnp.zeros((slot_count, lane), jnp.bfloat16).at[:, 0].set(p_col)
    x_padded = jnp.concatenate([x_tokens, jnp.zeros((1, model_width), jnp.bfloat16)], axis=0)
    dy_padded = jnp.concatenate([grad_out, jnp.zeros((1, model_width), jnp.bfloat16)], axis=0)
    packed = jnp.concatenate([x_padded[token_of], dy_padded[token_of], p_block], axis=1)
    dp_index = lax.axis_index("dp")
    shard_rows = w_gate.shape[1]
    pieces = ring_gather_pieces(jnp.stack([w_gate[0], w_up[0]]), "dp")
    packed, _ = lax.optimization_barrier((packed, pieces[-1]))
    arrived = lax.all_to_all(
        packed.reshape(n_expert, capacity, 2 * model_width + lane),
        "expert",
        split_axis=0,
        concat_axis=0,
        tiled=True,
    ).reshape(slot_count, 2 * model_width + lane)
    in_rows = arrived[:, :model_width]
    dy_rows = arrived[:, model_width : 2 * model_width]
    p_rows = arrived[:, 2 * model_width].astype(jnp.float32)
    scaled = (p_rows[:, None] * dy_rows.astype(jnp.float32)).astype(jnp.bfloat16)

    in_rot = roll_cols(in_rows, dp_index * shard_rows, model_width)
    group = 4 if len(pieces) % 4 == 0 else 2
    paired = [
        jnp.concatenate(pieces[k : k + group], axis=1) for k in range(0, len(pieces) - group + 1, group)
    ] + ([pieces[-1]] if len(pieces) % group else [])
    pair_rows = [p.shape[1] for p in paired]
    pair_start = [sum(pair_rows[:j]) for j in range(len(paired))]
    gate_pre = None
    up_pre = None
    for piece, lo, width in zip(paired, pair_start, pair_rows):
        cols = in_rot[:, lo : lo + width]
        g = jnp.dot(cols, piece[0], preferred_element_type=jnp.float32)
        u = jnp.dot(cols, piece[1], preferred_element_type=jnp.float32)
        gate_pre = g if gate_pre is None else gate_pre + g
        up_pre = u if up_pre is None else up_pre + u
    gate_sig = jax.nn.sigmoid(gate_pre)
    gate_act = gate_pre * gate_sig
    hidden = (gate_act * up_pre).astype(jnp.bfloat16)
    down_grad = lax.psum_scatter(
        lax.dot_general(
            scaled, hidden, (((0,), (0,)), ((), ())), preferred_element_type=jnp.float32
        ).astype(jnp.bfloat16),
        "dp",
        scatter_dimension=0,
        tiled=True,
    )
    grad_w_down = down_grad[None]
    piece_rows = lax.all_gather(w_down, "dp", axis=1, tiled=True)[0]
    out_piece = jnp.dot(hidden, piece_rows.T, preferred_element_type=jnp.float32)
    hidden_grad = jnp.dot(scaled, piece_rows, preferred_element_type=jnp.float32)
    prob_sum = jnp.sum(dy_rows.astype(jnp.float32) * out_piece, axis=1)
    up_grad = (hidden_grad * gate_act).astype(jnp.bfloat16)
    gate_grad = (hidden_grad * up_pre * gate_sig * (1.0 + gate_pre * (1.0 - gate_sig))).astype(
        jnp.bfloat16
    )
    x_grad_rot = jnp.concatenate(
        [
            (
                jnp.dot(gate_grad, piece[0].T, preferred_element_type=jnp.float32)
                + jnp.dot(up_grad, piece[1].T, preferred_element_type=jnp.float32)
            ).astype(jnp.bfloat16)
            for piece in paired
        ],
        axis=1,
    )
    x_grad = roll_cols(x_grad_rot, -dp_index * shard_rows, model_width)
    prob_block = jnp.zeros((slot_count, lane), jnp.bfloat16).at[:, 0].set(prob_sum.astype(jnp.bfloat16))
    returned = lax.all_to_all(
        jnp.concatenate([x_grad, prob_block], axis=1).reshape(n_expert, capacity, model_width + lane),
        "expert",
        split_axis=0,
        concat_axis=0,
        tiled=True,
    ).reshape(slot_count, model_width + lane)
    grad_slots = returned[:, :model_width]
    prob_slots = returned[:, model_width]
    picked = grad_slots[target].astype(jnp.float32).reshape(tok_count, top_count, model_width)
    grad_x = jnp.sum(picked, axis=1).astype(jnp.bfloat16)
    grad_probs = prob_slots[target].reshape(tok_count, top_count)
    return (grad_x, grad_probs, grad_w_down)


def solution(mesh):
    return jax.shard_map(
        per_device,
        mesh=mesh,
        in_specs=(
            P(("dp", "expert"), None),
            P(("dp", "expert"), None),
            P(("dp", "expert"), None),
            P(("dp", "expert"), None),
            P("expert", "dp", None),
            P("expert", "dp", None),
            P("expert", "dp", None),
        ),
        out_specs=(P(("dp", "expert"), None), P(("dp", "expert"), None), P("expert", "dp", None)),
        check_vma=False,
    )
```

```python
import jax
import jax.numpy as jnp
from jax import lax
from jax.sharding import PartitionSpec as P


def ring_gather_pieces(shard, axis):
    n = lax.axis_size(axis)
    fwd = [(m, (m + 1) % n) for m in range(n)]
    bwd = [(m, (m - 1) % n) for m in range(n)]
    nf = n // 2
    nb = (n - 1) // 2
    f = shard
    b = shard
    got_f = {}
    got_b = {}
    for s in range(1, nf + 1):
        f = lax.ppermute(f, axis, fwd)
        got_f[s] = f
        if s <= nb:
            b = lax.ppermute(b, axis, bwd)
            got_b[s] = b
    return [shard] + [got_b[k] for k in range(1, nb + 1)] + [got_f[n - k] for k in range(nb + 1, n)]


def roll_cols(a, shift, width):
    doubled = jnp.concatenate([a, a], axis=1)
    return lax.dynamic_slice_in_dim(doubled, shift % width, width, axis=1)


def per_device(x_tokens, grad_out, expert_ids, route_probs, w_gate, w_up, w_down):
    tok_count, model_width = x_tokens.shape
    top_count = expert_ids.shape[1]
    n_expert = lax.axis_size("expert")
    n_dp = lax.axis_size("dp")
    capacity = tok_count * top_count * 5 // (4 * n_expert)
    slot_count = n_expert * capacity
    routes = tok_count * top_count
    flat_ids = expert_ids.reshape(routes)
    onehot = (flat_ids[:, None] == jnp.arange(n_expert, dtype=jnp.int32)).astype(jnp.int32)
    route_rank = jnp.sum((jnp.cumsum(onehot, axis=0) - onehot) * onehot, axis=1)
    target = flat_ids * capacity + route_rank
    source = (
        jnp.full((slot_count,), routes, jnp.int32)
        .at[target]
        .set(jnp.arange(routes, dtype=jnp.int32))
    )
    token_of = jnp.where(source < routes, source // top_count, tok_count)
    lane = 128
    p_col = jnp.concatenate([route_probs.reshape(routes), jnp.zeros((1,), jnp.float32)]).astype(
        jnp.bfloat16
    )[source]
    p_block = jnp.zeros((slot_count, lane), jnp.bfloat16).at[:, 0].set(p_col)
    x_padded = jnp.concatenate([x_tokens, jnp.zeros((1, model_width), jnp.bfloat16)], axis=0)
    dy_padded = jnp.concatenate([grad_out, jnp.zeros((1, model_width), jnp.bfloat16)], axis=0)
    packed = jnp.concatenate([x_padded[token_of], dy_padded[token_of], p_block], axis=1)
    dp_index = lax.axis_index("dp")
    shard_rows = w_gate.shape[1]
    pieces = ring_gather_pieces(jnp.stack([w_gate[0], w_up[0]]), "dp")
    arrived = lax.all_to_all(
        packed.reshape(n_expert, capacity, 2 * model_width + lane),
        "expert",
        split_axis=0,
        concat_axis=0,
        tiled=True,
    ).reshape(slot_count, 2 * model_width + lane)
    in_rows = arrived[:, :model_width]
    dy_rows = arrived[:, model_width : 2 * model_width]
    p_rows = arrived[:, 2 * model_width].astype(jnp.float32)
    scaled = (p_rows[:, None] * dy_rows.astype(jnp.float32)).astype(jnp.bfloat16)

    in_rot = roll_cols(in_rows, dp_index * shard_rows, model_width)
    paired = [
        jnp.concatenate(pieces[k : k + 2], axis=1) for k in range(0, len(pieces) - 1, 2)
    ] + ([pieces[-1]] if len(pieces) % 2 else [])
    pair_rows = [p.shape[1] for p in paired]
    pair_start = [sum(pair_rows[:j]) for j in range(len(paired))]
    gate_pre = None
    up_pre = None
    for piece, lo, width in zip(paired, pair_start, pair_rows):
        cols = in_rot[:, lo : lo + width]
        g = jnp.dot(cols, piece[0], preferred_element_type=jnp.float32)
        u = jnp.dot(cols, piece[1], preferred_element_type=jnp.float32)
        gate_pre = g if gate_pre is None else gate_pre + g
        up_pre = u if up_pre is None else up_pre + u
    gate_sig = jax.nn.sigmoid(gate_pre)
    gate_act = gate_pre * gate_sig
    hidden = (gate_act * up_pre).astype(jnp.bfloat16)
    down_grad = lax.psum_scatter(
        lax.dot_general(
            scaled, hidden, (((0,), (0,)), ((), ())), preferred_element_type=jnp.float32
        ).astype(jnp.bfloat16),
        "dp",
        scatter_dimension=0,
        tiled=True,
    )
    grad_w_down = down_grad[None]
    piece_rows = lax.all_gather(w_down, "dp", axis=1, tiled=True)[0]
    out_piece = jnp.dot(hidden, piece_rows.T, preferred_element_type=jnp.float32)
    hidden_grad = jnp.dot(scaled, piece_rows, preferred_element_type=jnp.float32)
    prob_sum = jnp.sum(dy_rows.astype(jnp.float32) * out_piece, axis=1)
    up_grad = (hidden_grad * gate_act).astype(jnp.bfloat16)
    gate_grad = (hidden_grad * up_pre * gate_sig * (1.0 + gate_pre * (1.0 - gate_sig))).astype(
        jnp.bfloat16
    )
    x_grad_rot = jnp.concatenate(
        [
            (
                jnp.dot(gate_grad, piece[0].T, preferred_element_type=jnp.float32)
                + jnp.dot(up_grad, piece[1].T, preferred_element_type=jnp.float32)
            ).astype(jnp.bfloat16)
            for piece in paired
        ],
        axis=1,
    )
    x_grad = roll_cols(x_grad_rot, -dp_index * shard_rows, model_width)
    prob_block = jnp.zeros((slot_count, lane), jnp.bfloat16).at[:, 0].set(prob_sum.astype(jnp.bfloat16))
    returned = lax.all_to_all(
        jnp.concatenate([x_grad, prob_block], axis=1).reshape(n_expert, capacity, model_width + lane),
        "expert",
        split_axis=0,
        concat_axis=0,
        tiled=True,
    ).reshape(slot_count, model_width + lane)
    grad_slots = returned[:, :model_width]
    prob_slots = returned[:, model_width]
    picked = grad_slots[target].astype(jnp.float32).reshape(tok_count, top_count, model_width)
    grad_x = jnp.sum(picked, axis=1).astype(jnp.bfloat16)
    grad_probs = prob_slots[target].reshape(tok_count, top_count)
    return (grad_x, grad_probs, grad_w_down)


def solution(mesh):
    return jax.shard_map(
        per_device,
        mesh=mesh,
        in_specs=(
            P(("dp", "expert"), None),
            P(("dp", "expert"), None),
            P(("dp", "expert"), None),
            P(("dp", "expert"), None),
            P("expert", "dp", None),
            P("expert", "dp", None),
            P("expert", "dp", None),
        ),
        out_specs=(P(("dp", "expert"), None), P(("dp", "expert"), None), P("expert", "dp", None)),
        check_vma=False,
    )
```
